1024 devices in a mesh: ctx: 16 (over z, core), head: 8 (over y), dp: 8 (over x).
Axes of the slice: x: 8, y: 8, z: 8, core: 2. Of those that a mesh axis runs over, the one named last changes fastest.
Arguments:
- queries: bfloat16 [32768, 4096], P(('ctx', 'dp'), 'head'), may hold values from -4 to 4
- key_states: bfloat16 [32768, 1024], P(('ctx', 'dp'), 'head'), may hold values from -4 to 4
- value_states: bfloat16 [32768, 1024], P(('ctx', 'dp'), 'head'), may hold values from -4 to 4
- out_grad: bfloat16 [32768, 4096], P(('ctx', 'dp'), 'head'), may hold values from -24 to 24
- out_proj: bfloat16 [4096, 4096], P('head'), may hold values from -0.09375 to 0.09375
- local_span: int32 [256], P(('ctx', 'dp')), may hold values from 1 to 2
- stride_reach: int32 [256], P(('ctx', 'dp')), may hold values from 0 to 4
Outputs:
- d_queries: bfloat16 [32768, 4096], P(('ctx', 'dp'), 'head')
- d_keys: bfloat16 [32768, 1024], P(('ctx', 'dp'), 'head')
- d_values: bfloat16 [32768, 1024], P(('ctx', 'dp'), 'head')
- d_out_proj: float32 [4096, 4096], P(('head', 'dp'), 'ctx')
The draws below stay inside these ranges and needn't reach their ends.
All inputs are finite; a program needn't handle non-finite values.
Results may differ from the reference program's by a relative error of at most 0.017.
Values may be sent and summed in bfloat16 or wider, within the bound.
No kernel may reach another device: no remote copies, remote signals or barrier semaphores. Data moves between devices by JAX's collectives and lax.ppermute only.
A program may use at most 64 MiB of HBM per device.

```python
import math
import jax
import jax.numpy as jnp
from jax import lax

HD = 128
BLK = 128
QHEADS = 32
KV_HEADS = 8
DOUT = 4096
REACH = 4
LSPAN = 2
S_DEV = 256
SEQ = 32768
NBLK = 256
N_CTX = 16
N_DP = 8


def touch_ends(entries, stream_key, least, top_value):
    index_at = [jax.random.randint(jax.random.fold_in(stream_key, axis), (), 0, length) for axis, length in enumerate(entries.shape)]
    main_axis = entries.shape.index(max(entries.shape))
    neighbour = index_at[:main_axis] + [(index_at[main_axis] + 1) % entries.shape[main_axis]] + index_at[main_axis + 1:]
    return entries.at[tuple(index_at)].set(least).at[tuple(neighbour)].set(top_value)


def with_spikes(entries, stream_key, source, target, blocks, factor):
    owner, partner = [(jnp.arange(entries.shape[dim]) // (entries.shape[dim] // blocks)).reshape([-1 if axis == dim else 1 for axis in range(entries.ndim)]) for dim in (source, target)]
    chosen = jax.random.permutation(stream_key, blocks)[partner]
    strong = (owner == chosen) | (owner == (partner + blocks // 2) % blocks)
    return jnp.where(strong, factor * entries, entries)


def block_scale(own_key, dims, shards, smallest, high):
    loudness, own = 1.0, jax.random.fold_in(own_key, 6)
    for dim, blocks in shards:
        draws = jnp.exp(jax.random.uniform(jax.random.fold_in(own, dim), (blocks,), jnp.float32, smallest / len(shards), high / len(shards)))
        loudness = loudness * jnp.repeat(draws, dims[dim] // blocks).reshape([-1 if axis == dim else 1 for axis in range(len(dims))])
    return loudness


def normal_values(key, extent, width, bound, cuts=(), held_as=jnp.bfloat16):
    values = width * jax.random.normal(key, extent, jnp.float32)
    if cuts:
        values = values * block_scale(key, extent, cuts, -0.22, 0.18)
    return jnp.clip(values, -bound, bound).astype(held_as)


def gaussian_with(key, dims, width, most, split, heavy, kind=jnp.bfloat16):
    array = width * jax.random.normal(key, dims, jnp.float32)
    if split:
        array = array * block_scale(key, dims, split, -0.22, 0.18)
    return jnp.clip(with_spikes(array, jax.random.fold_in(key, 3), *heavy), -most, most).astype(kind)


def setup_inputs(seed: int = 0) -> dict:
    arg_keys = jax.random.split(jax.random.key(seed), 8)
    return {
        "queries": normal_values(arg_keys[0], (SEQ, QHEADS * HD), 1.6, 4.0, ((0, 128), (1, 8))),
        "key_states": normal_values(arg_keys[1], (SEQ, KV_HEADS * HD), 1.6, 4.0, ((0, 128), (1, 8))),
        "value_states": normal_values(arg_keys[2], (SEQ, KV_HEADS * HD), 1.0, 4.0, ((0, 128), (1, 8))),
        "out_grad": gaussian_with(arg_keys[3], (SEQ, DOUT), 1.0, 24.0, ((0, 128), (1, 8)), (0, 1, 128, 5.5)),
        "out_proj": normal_values(arg_keys[4], (QHEADS * HD, DOUT), (QHEADS * HD) ** -0.5, 0.09375, ((0, 8),)),
        "local_span": touch_ends(jax.random.randint(arg_keys[5], (NBLK,), 1, LSPAN + 1), jax.random.fold_in(arg_keys[5], 1), 1, LSPAN).astype(jnp.int32),
        "stride_reach": touch_ends(jax.random.randint(arg_keys[6], (NBLK,), 0, REACH + 1), jax.random.fold_in(arg_keys[6], 1), 0, REACH).astype(jnp.int32),
    }


def pair_masks(span_table, reaches, device, seq_rows, block, reach_count):
    stride = seq_rows // block
    positions = jnp.arange(seq_rows, dtype=jnp.int32)
    row_block = positions // block
    block_ids = jnp.arange(stride, dtype=jnp.int32)
    picked = row_block[:, None] == block_ids[None, :]
    span_row = lax.optimization_barrier(jnp.sum(jnp.where(picked, span_table[None, :], 0), axis=1, dtype=jnp.int32))
    reach_row = lax.optimization_barrier(jnp.sum(jnp.where(picked, reaches[None, :], 0), axis=1, dtype=jnp.int32))
    own_mask = (positions[None, :] <= positions[:, None]) & (row_block[None, :] >= row_block[:, None] - span_row[:, None] + 1)
    distances = jnp.arange(1, reach_count + 1, dtype=jnp.int32)
    query_block = device * stride + row_block
    far_block = device * stride - 1 - (distances - 1) * stride
    far_mask = (device >= distances)[None, :] & ((distances[None, :] <= reach_row[:, None]) | (far_block[None, :] >= query_block[:, None] - span_row[:, None] + 1))
    return jnp.concatenate([own_mask, jnp.repeat(far_mask, block, axis=1)], axis=1)

def attend_both(query_rows, key_rows, value_rows, grad_attended, allowed, kv_count, head_size):
    seq_rows = query_rows.shape[0]
    group_size = query_rows.shape[1] // (kv_count * head_size)
    scaling = 1.0 / math.sqrt(head_size)
    query_heads = query_rows.reshape(seq_rows, kv_count, group_size, head_size).astype(jnp.float32)
    key_heads = key_rows.reshape(-1, kv_count, head_size).astype(jnp.float32)
    value_heads = value_rows.reshape(-1, kv_count, head_size).astype(jnp.float32)
    grad_heads = grad_attended.reshape(seq_rows, kv_count, group_size, head_size).astype(jnp.float32)
    scores = jnp.einsum('skgd,tkd->kgst', query_heads, key_heads) * scaling
    raised = jnp.where(allowed, jnp.exp(scores), 0.0)
    weights = raised / lax.optimization_barrier(jnp.sum(raised, axis=-1, keepdims=True))
    rounded_weights = weights.astype(jnp.bfloat16)
    attended = jnp.einsum('kgst,tkd->skgd', rounded_weights.astype(jnp.float32), value_heads)
    attended = attended.astype(jnp.bfloat16).reshape(seq_rows, -1)
    d_weights = jnp.einsum('skgd,tkd->kgst', grad_heads, value_heads)
    row_dot = lax.optimization_barrier(jnp.sum(weights * d_weights, axis=-1, keepdims=True))
    d_scores = (weights * (d_weights - row_dot) * scaling).astype(jnp.bfloat16).astype(jnp.float32)
    d_query = jnp.einsum('kgst,tkd->skgd', d_scores, key_heads).astype(jnp.bfloat16).reshape(seq_rows, -1)
    d_key_all = jnp.einsum('kgst,skgd->tkd', d_scores, query_heads).reshape(-1, kv_count * head_size)
    d_value_all = jnp.einsum('kgst,skgd->tkd', rounded_weights.astype(jnp.float32), grad_heads).reshape(-1, kv_count * head_size)
    return (attended, d_query, d_key_all, d_value_all)

def reference(queries, key_states, value_states, out_grad, out_proj, local_span, stride_reach):
    stride = S_DEV // BLK
    kv_width = KV_HEADS * HD
    q_width = QHEADS * HD
    total_dev = N_DP * N_CTX
    key_arranged = key_states.reshape(total_dev, S_DEV, kv_width)
    value_arranged = value_states.reshape(total_dev, S_DEV, kv_width)

    def far_blocks(arranged):
        summary = arranged[:, S_DEV - BLK:]
        blanks = jnp.zeros((REACH, BLK, kv_width), arranged.dtype)
        padded = jnp.concatenate([blanks, summary], axis=0)
        stacked = jnp.stack([padded[REACH - distance:REACH - distance + total_dev] for distance in range(1, REACH + 1)], axis=1)
        return stacked.reshape(total_dev, REACH * BLK, kv_width)
    every_key = jnp.concatenate([key_arranged, far_blocks(key_arranged)], axis=1)
    every_value = jnp.concatenate([value_arranged, far_blocks(value_arranged)], axis=1)
    query_arranged = queries.reshape(total_dev, S_DEV, q_width)
    grad_arranged = out_grad.reshape(total_dev, S_DEV, DOUT)
    span_arranged = local_span.reshape(total_dev, stride)
    reach_arranged = stride_reach.reshape(total_dev, stride)
    devices = jnp.arange(total_dev, dtype=jnp.int32)

    def one_device(running, pieces):
        query_rows, key_rows, value_rows, grad_rows, span_table, reaches, device = pieces
        grad_attended = jnp.dot(grad_rows, out_proj.T, preferred_element_type=jnp.float32).astype(jnp.bfloat16)
        allowed = pair_masks(span_table, reaches, device, S_DEV, BLK, REACH)
        attended, d_query, d_key_all, d_value_all = attend_both(query_rows, key_rows, value_rows, grad_attended, allowed, KV_HEADS, HD)
        term_sum = jnp.dot(attended.T, grad_rows, preferred_element_type=jnp.float32)
        term_round = lax.optimization_barrier(term_sum.astype(jnp.bfloat16))
        return (running + term_round.astype(jnp.float32), (d_query, d_key_all, d_value_all))
    start_sum = jnp.zeros((q_width, DOUT), jnp.float32)
    d_out_proj, (d_query, d_key_all, d_value_all) = lax.scan(one_device, start_sum, (query_arranged, every_key, every_value, grad_arranged, span_arranged, reach_arranged, devices))

    def settle(d_all):
        own_part = d_all[:, :S_DEV]
        far_part = d_all[:, S_DEV:].reshape(total_dev, REACH, BLK, kv_width)
        returned = jnp.zeros((total_dev, BLK, kv_width), jnp.float32)
        for distance in range(1, REACH + 1):
            moved_part = jnp.concatenate([far_part[distance:, distance - 1], jnp.zeros((min(distance, total_dev), BLK, kv_width), jnp.float32)], axis=0)
            returned = returned + moved_part
        merged = jnp.concatenate([own_part[:, :S_DEV - BLK], own_part[:, S_DEV - BLK:] + returned], axis=1)
        return merged.astype(jnp.bfloat16).reshape(total_dev * S_DEV, kv_width)
    return (d_query.reshape(total_dev * S_DEV, q_width), settle(d_key_all), settle(d_value_all), d_out_proj)
```

```python
import math

import jax
import jax.numpy as jnp
from jax import lax
from jax.sharding import PartitionSpec as P

HD = 128
BLK = 128
REACH = 4


def passed_along(x, axis, by):
    peers = lax.axis_size(axis)
    pairs = [(i, i + by) for i in range(peers) if 0 <= i + by < peers]
    return lax.ppermute(x, axis, pairs)


def exchange_sum(x, axis):
    peers = lax.axis_size(axis)
    me = lax.axis_index(axis)
    levels = peers.bit_length() - 1
    rest = x.shape[1:]
    total = x.reshape((2,) * levels + (x.shape[0] // peers,) + rest)
    total = total.transpose(tuple(reversed(range(levels))) + tuple(range(levels, total.ndim)))
    total = total.reshape(x.shape)
    for level in range(levels):
        span = 1 << level
        half = total.shape[0] // 2
        upper = (me // span) % 2 == 1
        keep = jnp.where(upper, total[half:], total[:half])
        give = jnp.where(upper, total[:half], total[half:])
        total = keep + lax.ppermute(give, axis, [(i, i ^ span) for i in range(peers)])
    return total
def pair_masks(span_table, reaches, device, seq_rows, block, reach_count):
    stride = seq_rows // block
    positions = jnp.arange(seq_rows, dtype=jnp.int32)
    row_block = positions // block
    block_ids = jnp.arange(stride, dtype=jnp.int32)
    picked = row_block[:, None] == block_ids[None, :]
    span_row = jnp.sum(jnp.where(picked, span_table[None, :], 0), axis=1, dtype=jnp.int32)
    reach_row = jnp.sum(jnp.where(picked, reaches[None, :], 0), axis=1, dtype=jnp.int32)
    own_mask = (positions[None, :] <= positions[:, None]) & (
        row_block[None, :] >= row_block[:, None] - span_row[:, None] + 1
    )
    distances = jnp.arange(1, reach_count + 1, dtype=jnp.int32)
    query_block = device * stride + row_block
    far_block = device * stride - 1 - (distances - 1) * stride
    far_mask = (device >= distances)[None, :] & (
        (distances[None, :] <= reach_row[:, None])
        | (far_block[None, :] >= query_block[:, None] - span_row[:, None] + 1)
    )
    return jnp.concatenate([own_mask, jnp.repeat(far_mask, block, axis=1)], axis=1)


def attend_both(query_rows, key_rows, value_rows, grad_attended, allowed, kv_count, head_size):
    seq_rows = query_rows.shape[0]
    group_size = query_rows.shape[1] // (kv_count * head_size)
    scaling = 1.0 / math.sqrt(head_size)
    query_heads = query_rows.reshape(seq_rows, kv_count, group_size, head_size)
    key_heads = key_rows.reshape(-1, kv_count, head_size)
    value_heads = value_rows.reshape(-1, kv_count, head_size)
    grad_heads = grad_attended.reshape(seq_rows, kv_count, group_size, head_size)
    scores = (
        jnp.einsum("skgd,tkd->kgst", query_heads, key_heads, preferred_element_type=jnp.float32)
        * scaling
    )
    raised = jnp.where(allowed, jnp.exp(scores), 0.0)
    weights = raised / jnp.sum(raised, axis=-1, keepdims=True)
    rounded_weights = weights.astype(jnp.bfloat16)
    attended = jnp.einsum(
        "kgst,tkd->skgd", rounded_weights, value_heads, preferred_element_type=jnp.float32
    )
    attended = attended.astype(jnp.bfloat16).reshape(seq_rows, -1)
    d_weights = jnp.einsum(
        "skgd,tkd->kgst", grad_heads, value_heads, preferred_element_type=jnp.float32
    )
    row_dot = jnp.sum(weights * d_weights, axis=-1, keepdims=True)
    d_scores = (weights * (d_weights - row_dot) * scaling).astype(jnp.bfloat16)
    d_query = jnp.einsum("kgst,tkd->skgd", d_scores, key_heads, preferred_element_type=jnp.float32)
    d_query = d_query.astype(jnp.bfloat16).reshape(seq_rows, -1)
    d_key_all = jnp.einsum(
        "kgst,skgd->tkd", d_scores, query_heads, preferred_element_type=jnp.float32
    ).reshape(-1, kv_count * head_size)
    d_value_all = jnp.einsum(
        "kgst,skgd->tkd", rounded_weights, grad_heads, preferred_element_type=jnp.float32
    ).reshape(-1, kv_count * head_size)
    return (attended, d_query, d_key_all, d_value_all)


def local(queries, key_states, value_states, out_grad, out_proj, local_span, stride_reach):
    seq_rows = key_states.shape[0]
    kv_width = key_states.shape[1]
    kv_count = kv_width // HD
    device = lax.axis_index(("ctx", "dp"))
    summary = jnp.concatenate(
        [key_states[seq_rows - BLK :], value_states[seq_rows - BLK :]], axis=1
    )
    far_key_list = []
    far_value_list = []
    for distance in range(1, REACH + 1):
        moved = passed_along(summary, ("ctx", "dp"), distance)
        far_key_list.append(moved[:, :kv_width])
        far_value_list.append(moved[:, kv_width:])
    all_keys = jnp.concatenate([key_states] + far_key_list, axis=0)
    all_values = jnp.concatenate([value_states] + far_value_list, axis=0)
    grad_rows = lax.all_gather(out_grad, "head", axis=1, tiled=True)
    grad_attended = lax.dot_general(
        grad_rows, out_proj, (((1,), (1,)), ((), ())), preferred_element_type=jnp.float32
    ).astype(jnp.bfloat16)
    allowed = pair_masks(local_span, stride_reach, device, seq_rows, BLK, REACH)
    attended, d_query, d_key_all, d_value_all = attend_both(
        queries, all_keys, all_values, grad_attended, allowed, kv_count, HD
    )
    returned_keys = jnp.zeros((BLK, kv_width), jnp.float32)
    returned_values = jnp.zeros((BLK, kv_width), jnp.float32)
    for distance in range(1, REACH + 1):
        lower = seq_rows + (distance - 1) * BLK
        back = passed_along(
            jnp.concatenate(
                [d_key_all[lower : lower + BLK], d_value_all[lower : lower + BLK]], axis=1
            ),
            ("ctx", "dp"),
            -distance,
        )
        returned_keys = returned_keys + back[:, :kv_width]
        returned_values = returned_values + back[:, kv_width:]
    d_keys = jnp.concatenate(
        [d_key_all[: seq_rows - BLK], d_key_all[seq_rows - BLK : seq_rows] + returned_keys], axis=0
    ).astype(jnp.bfloat16)
    d_values = jnp.concatenate(
        [d_value_all[: seq_rows - BLK], d_value_all[seq_rows - BLK : seq_rows] + returned_values],
        axis=0,
    ).astype(jnp.bfloat16)
    partial_cols = lax.psum_scatter(
        lax.dot_general(
            grad_rows, attended, (((0,), (0,)), ((), ())), preferred_element_type=jnp.float32
        ).astype(jnp.bfloat16),
        "ctx",
        scatter_dimension=0,
        tiled=True,
    ).astype(jnp.float32)
    d_out_proj = exchange_sum(partial_cols.T, "dp")
    return (d_query, d_keys, d_values, d_out_proj)


def solution(mesh):
    in_specs = (
        P(("ctx", "dp"), "head"),
        P(("ctx", "dp"), "head"),
        P(("ctx", "dp"), "head"),
        P(("ctx", "dp"), "head"),
        P("head", None),
        P(("ctx", "dp")),
        P(("ctx", "dp")),
    )
    out_specs = (
        P(("ctx", "dp"), "head"),
        P(("ctx", "dp"), "head"),
        P(("ctx", "dp"), "head"),
        P(("head", "dp"), "ctx"),
    )
    return jax.shard_map(local, mesh=mesh, in_specs=in_specs, out_specs=out_specs, check_vma=False)
```

```python
import math

import jax
import jax.numpy as jnp
from jax import lax
from jax.sharding import PartitionSpec as P

HD = 128
BLK = 128
REACH = 4
CTX = ("z", "core")


def passed_along(x, axis, by):
    peers = lax.axis_size(axis)
    pairs = [(i, i + by) for i in range(peers) if 0 <= i + by < peers]
    return lax.ppermute(x, axis, pairs)


def exchange_sum(x, axis):
    peers = lax.axis_size(axis)
    me = lax.axis_index(axis)
    levels = peers.bit_length() - 1
    rest = x.shape[1:]
    total = x.reshape((2,) * levels + (x.shape[0] // peers,) + rest)
    total = total.transpose(tuple(reversed(range(levels))) + tuple(range(levels, total.ndim)))
    total = total.reshape(x.shape)
    for level in range(levels):
        span = 1 << level
        half = total.shape[0] // 2
        upper = (me // span) % 2 == 1
        keep = jnp.where(upper, total[half:], total[:half])
        give = jnp.where(upper, total[:half], total[half:])
        total = keep + lax.ppermute(give, axis, [(i, i ^ span) for i in range(peers)])
    return total
def pair_masks(span_table, reaches, device, seq_rows, block, reach_count):
    stride = seq_rows // block
    positions = jnp.arange(seq_rows, dtype=jnp.int32)
    row_block = positions // block
    block_ids = jnp.arange(stride, dtype=jnp.int32)
    picked = row_block[:, None] == block_ids[None, :]
    span_row = jnp.sum(jnp.where(picked, span_table[None, :], 0), axis=1, dtype=jnp.int32)
    reach_row = jnp.sum(jnp.where(picked, reaches[None, :], 0), axis=1, dtype=jnp.int32)
    own_mask = (positions[None, :] <= positions[:, None]) & (
        row_block[None, :] >= row_block[:, None] - span_row[:, None] + 1
    )
    distances = jnp.arange(1, reach_count + 1, dtype=jnp.int32)
    query_block = device * stride + row_block
    far_block = device * stride - 1 - (distances - 1) * stride
    far_mask = (device >= distances)[None, :] & (
        (distances[None, :] <= reach_row[:, None])
        | (far_block[None, :] >= query_block[:, None] - span_row[:, None] + 1)
    )
    return jnp.concatenate([own_mask, jnp.repeat(far_mask, block, axis=1)], axis=1)


def attend_both(query_rows, key_rows, value_rows, grad_attended, allowed, kv_count, head_size):
    seq_rows = query_rows.shape[0]
    group_size = query_rows.shape[1] // (kv_count * head_size)
    scaling = 1.0 / math.sqrt(head_size)
    query_heads = query_rows.reshape(seq_rows, kv_count, group_size, head_size)
    key_heads = key_rows.reshape(-1, kv_count, head_size)
    value_heads = value_rows.reshape(-1, kv_count, head_size)
    grad_heads = grad_attended.reshape(seq_rows, kv_count, group_size, head_size)
    scores = (
        jnp.einsum("skgd,tkd->kgst", query_heads, key_heads, preferred_element_type=jnp.float32)
        * scaling
    )
    raised = jnp.where(allowed, jnp.exp(scores), 0.0)
    weights = raised / jnp.sum(raised, axis=-1, keepdims=True)
    rounded_weights = weights.astype(jnp.bfloat16)
    attended = jnp.einsum(
        "kgst,tkd->skgd", rounded_weights, value_heads, preferred_element_type=jnp.float32
    )
    attended = attended.astype(jnp.bfloat16).reshape(seq_rows, -1)
    d_weights = jnp.einsum(
        "skgd,tkd->kgst", grad_heads, value_heads, preferred_element_type=jnp.float32
    )
    row_dot = jnp.sum(weights * d_weights, axis=-1, keepdims=True)
    d_scores = (weights * (d_weights - row_dot) * scaling).astype(jnp.bfloat16)
    d_query = jnp.einsum("kgst,tkd->skgd", d_scores, key_heads, preferred_element_type=jnp.float32)
    d_query = d_query.astype(jnp.bfloat16).reshape(seq_rows, -1)
    d_key_all = jnp.einsum(
        "kgst,skgd->tkd", d_scores, query_heads, preferred_element_type=jnp.float32
    ).reshape(-1, kv_count * head_size)
    d_value_all = jnp.einsum(
        "kgst,skgd->tkd", rounded_weights, grad_heads, preferred_element_type=jnp.float32
    ).reshape(-1, kv_count * head_size)
    return (attended, d_query, d_key_all, d_value_all)


def local(queries, key_states, value_states, out_grad, out_proj, local_span, stride_reach):
    seq_rows = key_states.shape[0]
    kv_width = key_states.shape[1]
    kv_count = kv_width // HD
    device = lax.axis_index(CTX + ("dp",))
    summary = jnp.concatenate(
        [key_states[seq_rows - BLK :], value_states[seq_rows - BLK :]], axis=1
    )
    far_key_list = []
    far_value_list = []
    for distance in range(1, REACH + 1):
        moved = passed_along(summary, CTX + ("dp",), distance)
        far_key_list.append(moved[:, :kv_width])
        far_value_list.append(moved[:, kv_width:])
    all_keys = jnp.concatenate([key_states] + far_key_list, axis=0)
    all_values = jnp.concatenate([value_states] + far_value_list, axis=0)
    grad_rows = lax.all_gather(out_grad, "head", axis=1, tiled=True)
    grad_attended = lax.dot_general(
        grad_rows, out_proj, (((1,), (1,)), ((), ())), preferred_element_type=jnp.float32
    ).astype(jnp.bfloat16)
    allowed = pair_masks(local_span, stride_reach, device, seq_rows, BLK, REACH)
    attended, d_query, d_key_all, d_value_all = attend_both(
        queries, all_keys, all_values, grad_attended, allowed, kv_count, HD
    )
    returned_keys = jnp.zeros((BLK, kv_width), jnp.float32)
    returned_values = jnp.zeros((BLK, kv_width), jnp.float32)
    for distance in range(1, REACH + 1):
        lower = seq_rows + (distance - 1) * BLK
        back = passed_along(
            jnp.concatenate(
                [d_key_all[lower : lower + BLK], d_value_all[lower : lower + BLK]], axis=1
            ),
            CTX + ("dp",),
            -distance,
        )
        returned_keys = returned_keys + back[:, :kv_width]
        returned_values = returned_values + back[:, kv_width:]
    d_keys = jnp.concatenate(
        [d_key_all[: seq_rows - BLK], d_key_all[seq_rows - BLK : seq_rows] + returned_keys], axis=0
    ).astype(jnp.bfloat16)
    d_values = jnp.concatenate(
        [d_value_all[: seq_rows - BLK], d_value_all[seq_rows - BLK : seq_rows] + returned_values],
        axis=0,
    ).astype(jnp.bfloat16)
    term = lax.dot_general(
        grad_rows, attended, (((0,), (0,)), ((), ())), preferred_element_type=jnp.float32
    ).astype(jnp.bfloat16)
    chip_cols = lax.psum_scatter(term, "z", scatter_dimension=0, tiled=True).astype(jnp.float32)
    half = chip_cols.shape[0] // 2
    upper = lax.axis_index("core") == 1
    kept = jnp.where(upper, chip_cols[half:], chip_cols[:half])
    given = jnp.where(upper, chip_cols[:half], chip_cols[half:])
    partial_cols = kept + lax.ppermute(given, "core", [(0, 1), (1, 0)])
    d_out_proj = exchange_sum(partial_cols.T, "dp")
    return (d_query, d_keys, d_values, d_out_proj)


def solution(mesh):
    devices = mesh.devices
    split = jax.sharding.Mesh(
        devices.reshape(devices.shape[0] // 2, 2, *devices.shape[1:]),
        CTX + mesh.axis_names[1:],
    )
    rows = CTX + ("dp",)
    in_specs = (
        P(rows, "head"),
        P(rows, "head"),
        P(rows, "head"),
        P(rows, "head"),
        P("head", None),
        P(rows),
        P(rows),
    )
    out_specs = (
        P(rows, "head"),
        P(rows, "head"),
        P(rows, "head"),
        P(("head", "dp"), CTX),
    )
    return jax.shard_map(local, mesh=split, in_specs=in_specs, out_specs=out_specs, check_vma=False)
```

```python
import math

import jax
import jax.numpy as jnp
from jax import lax
from jax.sharding import PartitionSpec as P

HD = 128
BLK = 128
REACH = 4
CTX = ("z", "core")


def passed_along(x, axis, by):
    peers = lax.axis_size(axis)
    pairs = [(i, i + by) for i in range(peers) if 0 <= i + by < peers]
    return lax.ppermute(x, axis, pairs)


def exchange_sum(x, axis):
    peers = lax.axis_size(axis)
    me = lax.axis_index(axis)
    levels = peers.bit_length() - 1
    rest = x.shape[1:]
    total = x.reshape((2,) * levels + (x.shape[0] // peers,) + rest)
    total = total.transpose(tuple(reversed(range(levels))) + tuple(range(levels, total.ndim)))
    total = total.reshape(x.shape)
    for level in range(levels):
        span = 1 << level
        half = total.shape[0] // 2
        upper = (me // span) % 2 == 1
        keep = jnp.where(upper, total[half:], total[:half])
        give = jnp.where(upper, total[:half], total[half:])
        total = keep + lax.ppermute(give, axis, [(i, i ^ span) for i in range(peers)])
    return total
def pair_masks(span_table, reaches, device, seq_rows, block, reach_count):
    stride = seq_rows // block
    positions = jnp.arange(seq_rows, dtype=jnp.int32)
    row_block = positions // block
    block_ids = jnp.arange(stride, dtype=jnp.int32)
    picked = row_block[:, None] == block_ids[None, :]
    span_row = jnp.sum(jnp.where(picked, span_table[None, :], 0), axis=1, dtype=jnp.int32)
    reach_row = jnp.sum(jnp.where(picked, reaches[None, :], 0), axis=1, dtype=jnp.int32)
    own_mask = (positions[None, :] <= positions[:, None]) & (
        row_block[None, :] >= row_block[:, None] - span_row[:, None] + 1
    )
    distances = jnp.arange(1, reach_count + 1, dtype=jnp.int32)
    query_block = device * stride + row_block
    far_block = device * stride - 1 - (distances - 1) * stride
    far_mask = (device >= distances)[None, :] & (
        (distances[None, :] <= reach_row[:, None])
        | (far_block[None, :] >= query_block[:, None] - span_row[:, None] + 1)
    )
    return jnp.concatenate([own_mask, jnp.repeat(far_mask, block, axis=1)], axis=1)


def attend_both(query_rows, key_rows, value_rows, grad_attended, allowed, kv_count, head_size):
    seq_rows = query_rows.shape[0]
    group_size = query_rows.shape[1] // (kv_count * head_size)
    scaling = 1.0 / math.sqrt(head_size)
    query_heads = query_rows.reshape(seq_rows, kv_count, group_size, head_size)
    key_heads = key_rows.reshape(-1, kv_count, head_size)
    value_heads = value_rows.reshape(-1, kv_count, head_size)
    grad_heads = grad_attended.reshape(seq_rows, kv_count, group_size, head_size)
    scores = (
        jnp.einsum("skgd,tkd->kgst", query_heads, key_heads, preferred_element_type=jnp.float32)
        * scaling
    )
    raised = jnp.where(allowed, jnp.exp(scores), 0.0)
    weights = raised / jnp.sum(raised, axis=-1, keepdims=True)
    rounded_weights = weights.astype(jnp.bfloat16)
    attended = jnp.einsum(
        "kgst,tkd->skgd", rounded_weights, value_heads, preferred_element_type=jnp.float32
    )
    attended = attended.astype(jnp.bfloat16).reshape(seq_rows, -1)
    d_weights = jnp.einsum(
        "skgd,tkd->kgst", grad_heads, value_heads, preferred_element_type=jnp.float32
    )
    row_dot = jnp.sum(weights * d_weights, axis=-1, keepdims=True)
    d_scores = (weights * (d_weights - row_dot) * scaling).astype(jnp.bfloat16)
    d_query = jnp.einsum("kgst,tkd->skgd", d_scores, key_heads, preferred_element_type=jnp.float32)
    d_query = d_query.astype(jnp.bfloat16).reshape(seq_rows, -1)
    d_key_all = jnp.einsum(
        "kgst,skgd->tkd", d_scores, query_heads, preferred_element_type=jnp.float32
    ).reshape(-1, kv_count * head_size)
    d_value_all = jnp.einsum(
        "kgst,skgd->tkd", rounded_weights, grad_heads, preferred_element_type=jnp.float32
    ).reshape(-1, kv_count * head_size)
    return (attended, d_query, d_key_all, d_value_all)


def local(queries, key_states, value_states, out_grad, out_proj, local_span, stride_reach):
    seq_rows = key_states.shape[0]
    kv_width = key_states.shape[1]
    kv_count = kv_width // HD
    device = lax.axis_index(CTX + ("dp",))
    summary = jnp.concatenate(
        [key_states[seq_rows - BLK :], value_states[seq_rows - BLK :]], axis=1
    )
    far_key_list = []
    far_value_list = []
    for distance in range(1, REACH + 1):
        moved = passed_along(summary, CTX + ("dp",), distance)
        far_key_list.append(moved[:, :kv_width])
        far_value_list.append(moved[:, kv_width:])
    all_keys = jnp.concatenate([key_states] + far_key_list, axis=0)
    all_values = jnp.concatenate([value_states] + far_value_list, axis=0)
    grad_rows = lax.all_gather(out_grad, "head", axis=1, tiled=True)
    grad_attended = lax.dot_general(
        grad_rows, out_proj, (((1,), (1,)), ((), ())), preferred_element_type=jnp.float32
    ).astype(jnp.bfloat16)
    allowed = pair_masks(local_span, stride_reach, device, seq_rows, BLK, REACH)
    attended, d_query, d_key_all, d_value_all = attend_both(
        queries, all_keys, all_values, grad_attended, allowed, kv_count, HD
    )
    returned_keys = jnp.zeros((BLK, kv_width), jnp.float32)
    returned_values = jnp.zeros((BLK, kv_width), jnp.float32)
    for distance in range(1, REACH + 1):
        lower = seq_rows + (distance - 1) * BLK
        back = passed_along(
            jnp.concatenate(
                [d_key_all[lower : lower + BLK], d_value_all[lower : lower + BLK]], axis=1
            ),
            CTX + ("dp",),
            -distance,
        )
        returned_keys = returned_keys + back[:, :kv_width]
        returned_values = returned_values + back[:, kv_width:]
    d_keys = jnp.concatenate(
        [d_key_all[: seq_rows - BLK], d_key_all[seq_rows - BLK : seq_rows] + returned_keys], axis=0
    ).astype(jnp.bfloat16)
    d_values = jnp.concatenate(
        [d_value_all[: seq_rows - BLK], d_value_all[seq_rows - BLK : seq_rows] + returned_values],
        axis=0,
    ).astype(jnp.bfloat16)
    term = lax.dot_general(
        grad_rows, attended, (((0,), (0,)), ((), ())), preferred_element_type=jnp.float32
    ).astype(jnp.bfloat16)
    chip_cols = lax.psum_scatter(term, "z", scatter_dimension=0, tiled=True).astype(jnp.float32)
    chip_cols, d_keys, d_values = lax.optimization_barrier((chip_cols, d_keys, d_values))
    half = chip_cols.shape[0] // 2
    upper = lax.axis_index("core") == 1
    kept = jnp.where(upper, chip_cols[half:], chip_cols[:half])
    given = jnp.where(upper, chip_cols[:half], chip_cols[half:])
    partial_cols = kept + lax.ppermute(given, "core", [(0, 1), (1, 0)])
    d_out_proj = exchange_sum(partial_cols.T, "dp")
    return (d_query, d_keys, d_values, d_out_proj)


def solution(mesh):
    devices = mesh.devices
    split = jax.sharding.Mesh(
        devices.reshape(devices.shape[0] // 2, 2, *devices.shape[1:]),
        CTX + mesh.axis_names[1:],
    )
    rows = CTX + ("dp",)
    in_specs = (
        P(rows, "head"),
        P(rows, "head"),
        P(rows, "head"),
        P(rows, "head"),
        P("head", None),
        P(rows),
        P(rows),
    )
    out_specs = (
        P(rows, "head"),
        P(rows, "head"),
        P(rows, "head"),
        P(("head", "dp"), CTX),
    )
    return jax.shard_map(local, mesh=split, in_specs=in_specs, out_specs=out_specs, check_vma=False)
```

```python
import math

import jax
import jax.numpy as jnp
from jax import lax
from jax.sharding import PartitionSpec as P

HD = 128
BLK = 128
REACH = 4


def passed_along(x, axis, by):
    peers = lax.axis_size(axis)
    pairs = [(i, i + by) for i in range(peers) if 0 <= i + by < peers]
    return lax.ppermute(x, axis, pairs)


def exchange_sum(x, axis):
    peers = lax.axis_size(axis)
    me = lax.axis_index(axis)
    levels = peers.bit_length() - 1
    rest = x.shape[1:]
    total = x.reshape((2,) * levels + (x.shape[0] // peers,) + rest)
    total = total.transpose(tuple(reversed(range(levels))) + tuple(range(levels, total.ndim)))
    total = total.reshape(x.shape)
    for level in range(levels):
        span = 1 << level
        half = total.shape[0] // 2
        upper = (me // span) % 2 == 1
        keep = jnp.where(upper, total[half:], total[:half])
        give = jnp.where(upper, total[:half], total[half:])
        total = keep + lax.ppermute(give, axis, [(i, i ^ span) for i in range(peers)])
    return total
def pair_masks(span_table, reaches, device, seq_rows, block, reach_count):
    stride = seq_rows // block
    positions = jnp.arange(seq_rows, dtype=jnp.int32)
    row_block = positions // block
    block_ids = jnp.arange(stride, dtype=jnp.int32)
    picked = row_block[:, None] == block_ids[None, :]
    span_row = jnp.sum(jnp.where(picked, span_table[None, :], 0), axis=1, dtype=jnp.int32)
    reach_row = jnp.sum(jnp.where(picked, reaches[None, :], 0), axis=1, dtype=jnp.int32)
    own_mask = (positions[None, :] <= positions[:, None]) & (
        row_block[None, :] >= row_block[:, None] - span_row[:, None] + 1
    )
    distances = jnp.arange(1, reach_count + 1, dtype=jnp.int32)
    query_block = device * stride + row_block
    far_block = device * stride - 1 - (distances - 1) * stride
    far_mask = (device >= distances)[None, :] & (
        (distances[None, :] <= reach_row[:, None])
        | (far_block[None, :] >= query_block[:, None] - span_row[:, None] + 1)
    )
    return jnp.concatenate([own_mask, jnp.repeat(far_mask, block, axis=1)], axis=1)


def attend_both(query_rows, key_rows, value_rows, grad_attended, allowed, kv_count, head_size):
    seq_rows = query_rows.shape[0]
    group_size = query_rows.shape[1] // (kv_count * head_size)
    scaling = 1.0 / math.sqrt(head_size)
    query_heads = query_rows.reshape(seq_rows, kv_count, group_size, head_size)
    key_heads = key_rows.reshape(-1, kv_count, head_size)
    value_heads = value_rows.reshape(-1, kv_count, head_size)
    grad_heads = grad_attended.reshape(seq_rows, kv_count, group_size, head_size)
    scores = (
        jnp.einsum("skgd,tkd->kgst", query_heads, key_heads, preferred_element_type=jnp.float32)
        * scaling
    )
    raised = jnp.where(allowed, jnp.exp(scores), 0.0)
    weights = raised / jnp.sum(raised, axis=-1, keepdims=True)
    rounded_weights = weights.astype(jnp.bfloat16)
    attended = jnp.einsum(
        "kgst,tkd->skgd", rounded_weights, value_heads, preferred_element_type=jnp.float32
    )
    attended = attended.astype(jnp.bfloat16).reshape(seq_rows, -1)
    d_weights = jnp.einsum(
        "skgd,tkd->kgst", grad_heads, value_heads, preferred_element_type=jnp.float32
    )
    row_dot = jnp.sum(weights * d_weights, axis=-1, keepdims=True)
    d_scores = (weights * (d_weights - row_dot) * scaling).astype(jnp.bfloat16)
    d_query = jnp.einsum("kgst,tkd->skgd", d_scores, key_heads, preferred_element_type=jnp.float32)
    d_query = d_query.astype(jnp.bfloat16).reshape(seq_rows, -1)
    d_key_all = jnp.einsum(
        "kgst,skgd->tkd", d_scores, query_heads, preferred_element_type=jnp.float32
    ).reshape(-1, kv_count * head_size)
    d_value_all = jnp.einsum(
        "kgst,skgd->tkd", rounded_weights, grad_heads, preferred_element_type=jnp.float32
    ).reshape(-1, kv_count * head_size)
    return (attended, d_query, d_key_all, d_value_all)


def local(queries, key_states, value_states, out_grad, out_proj, local_span, stride_reach):
    seq_rows = key_states.shape[0]
    kv_width = key_states.shape[1]
    kv_count = kv_width // HD
    device = lax.axis_index(("ctx", "dp"))
    summary = jnp.concatenate(
        [key_states[seq_rows - BLK :], value_states[seq_rows - BLK :]], axis=1
    )
    far_key_list = []
    far_value_list = []
    for distance in range(1, REACH + 1):
        moved = passed_along(summary, ("ctx", "dp"), distance)
        far_key_list.append(moved[:, :kv_width])
        far_value_list.append(moved[:, kv_width:])
    all_keys = jnp.concatenate([key_states] + far_key_list, axis=0)
    all_values = jnp.concatenate([value_states] + far_value_list, axis=0)
    grad_rows = lax.all_gather(out_grad, "head", axis=1, tiled=True)
    grad_attended = lax.dot_general(
        grad_rows, out_proj, (((1,), (1,)), ((), ())), preferred_element_type=jnp.float32
    ).astype(jnp.bfloat16)
    allowed = pair_masks(local_span, stride_reach, device, seq_rows, BLK, REACH)
    attended, d_query, d_key_all, d_value_all = attend_both(
        queries, all_keys, all_values, grad_attended, allowed, kv_count, HD
    )
    returned_keys = jnp.zeros((BLK, kv_width), jnp.float32)
    returned_values = jnp.zeros((BLK, kv_width), jnp.float32)
    for distance in range(1, REACH + 1):
        lower = seq_rows + (distance - 1) * BLK
        back = passed_along(
            jnp.concatenate(
                [d_key_all[lower : lower + BLK], d_value_all[lower : lower + BLK]], axis=1
            ),
            ("ctx", "dp"),
            -distance,
        )
        returned_keys = returned_keys + back[:, :kv_width]
        returned_values = returned_values + back[:, kv_width:]
    d_keys = jnp.concatenate(
        [d_key_all[: seq_rows - BLK], d_key_all[seq_rows - BLK : seq_rows] + returned_keys], axis=0
    ).astype(jnp.bfloat16)
    d_values = jnp.concatenate(
        [d_value_all[: seq_rows - BLK], d_value_all[seq_rows - BLK : seq_rows] + returned_values],
        axis=0,
    ).astype(jnp.bfloat16)
    partial_cols = lax.psum_scatter(
        lax.dot_general(
            grad_rows, attended, (((0,), (0,)), ((), ())), preferred_element_type=jnp.float32
        ).astype(jnp.bfloat16),
        "ctx",
        scatter_dimension=0,
        tiled=True,
    ).astype(jnp.float32)
    partial_cols, d_keys, d_values = lax.optimization_barrier((partial_cols, d_keys, d_values))
    d_out_proj = exchange_sum(partial_cols.T, "dp")
    return (d_query, d_keys, d_values, d_out_proj)


def solution(mesh):
    in_specs = (
        P(("ctx", "dp"), "head"),
        P(("ctx", "dp"), "head"),
        P(("ctx", "dp"), "head"),
        P(("ctx", "dp"), "head"),
        P("head", None),
        P(("ctx", "dp")),
        P(("ctx", "dp")),
    )
    out_specs = (
        P(("ctx", "dp"), "head"),
        P(("ctx", "dp"), "head"),
        P(("ctx", "dp"), "head"),
        P(("head", "dp"), "ctx"),
    )
    return jax.shard_map(local, mesh=mesh, in_specs=in_specs, out_specs=out_specs, check_vma=False)
```
